256 devices in a mesh: row: 32 (over z, y_hi, core), col: 8 (over x, y_lo).
Axes of the slice: x: 4, y: 4 (y_hi: 2, y_lo: 2; y = y_hi * 2 + y_lo), z: 8, core: 2. Of those that a mesh axis runs over, the one named last changes fastest.
Arguments:
- affinity_tiles: bfloat16 [1024, 512, 512], P(('row', 'col')), may hold values from -6 to 6
- tile_rows: int32 [1024], P(('row', 'col')), may hold values from -1 to 63, as said below
- tile_cols: int32 [1024], P(('row', 'col')), may hold values from -1 to 63, as said below
- lang_counts: int32 [32], replicated, may hold values from 1 to 8192, 32768 in all
- start_basis: float32 [8, 4096, 64], P('col', 'row'), may hold values from -6 to 6
Outputs:
- eigen_basis: float32 [8, 4096, 64], P('col', 'row')
The draws below stay inside these ranges and needn't reach their ends.
Inputs may be any that keep to these rules, and one draw needn't show every extreme that they name: `tile_rows`: the slots of device (r, c) are entries (r * 8 + c) * 4 onward of both lists. Every used slot names a distinct block with block row from r * 2 to (r + 1) * 2 - 1, block column from c * 8 to (c + 1) * 8 - 1, and block row <= block column; no block is named twice. Empty slots hold -1 in both lists and come after the used slots of their device. Device (0, 7) uses all 4 slots. `tile_cols`: same slots as tile_rows.
All inputs are finite; a program needn't handle non-finite values.
Results may differ from the reference program's by a relative error of at most 0.0044.
Values may be sent and summed in bfloat16 or wider, within the bound.
No kernel may reach another device: no remote copies, remote signals or barrier semaphores. Data moves between devices by JAX's collectives and lax.ppermute only.
A program may use at most 64 MiB of HBM per device.

```python
import math
import jax
import jax.numpy as jnp
import numpy as np
from jax import lax

TILE = 512
VECTORS = 64
ROW_BLOCKS = 2
TILES_DEV = 4
LANGS = 32
ITERS = 3
GRID_ROWS = 32
GRID_COLS = 8
BLOCKS = 64
COL_BLOCKS = 8
DOCS = 32768
COL_DOCS = 4096
TILES = 1024


def tile_layout(key):
    layout_key = jax.random.fold_in(key, 17)
    cell_count = ROW_BLOCKS * COL_BLOCKS

    def one_device(device):
        device_key = jax.random.fold_in(layout_key, device)
        row_group = device // GRID_COLS
        col_group = device % GRID_COLS
        cell_ids = jnp.arange(cell_count, dtype=jnp.int32)
        block_row = row_group * ROW_BLOCKS + cell_ids // COL_BLOCKS
        block_col = col_group * COL_BLOCKS + cell_ids % COL_BLOCKS
        upper = (block_row <= block_col).astype(jnp.int32)
        shuffle = jax.random.permutation(jax.random.fold_in(device_key, 1), cell_count).astype(jnp.int32)
        sort_key = (1 - upper) * cell_count + shuffle
        ranked = jnp.argsort(sort_key, stable=True)
        available = jnp.sum(upper)
        wanted = jax.random.randint(jax.random.fold_in(device_key, 2), (), TILES_DEV // 2, TILES_DEV + 1)
        wanted = jnp.where(device == GRID_COLS - 1, TILES_DEV, wanted)
        used = jnp.minimum(available, wanted)
        chosen = ranked[:TILES_DEV]
        slot_ids = jnp.arange(TILES_DEV, dtype=jnp.int32)
        in_use = slot_ids < used
        row_list = jnp.where(in_use, block_row[chosen], -1).astype(jnp.int32)
        col_list = jnp.where(in_use, block_col[chosen], -1).astype(jnp.int32)
        return (row_list, col_list)
    row_all, col_all = jax.vmap(one_device)(jnp.arange(GRID_ROWS * GRID_COLS, dtype=jnp.int32))
    return (row_all.reshape(-1), col_all.reshape(-1))


def draw_tile_rows(key, part):
    return tile_layout(key)[0]


def draw_tile_cols(key, part):
    return tile_layout(key)[1]


def block_levels(rng, dims, shards, low, high):
    level = 1.0
    for dim, shards_of in shards:
        draws = jax.random.uniform(jax.random.fold_in(jax.random.fold_in(rng, 6), dim), (shards_of,), jnp.float32, low / len(shards), high / len(shards))
        level = level * jnp.repeat(jnp.exp(draws), dims[dim] // shards_of).reshape((-1,) + (1,) * (len(dims) - 1 - dim))
    return level


def length_profile(number_of, total, reach, slope):
    loads = [(1 << 20) // math.isqrt(grade ** slope) + 1 for grade in range(2, number_of + 1)]
    rest, counts = total - reach - (number_of - 1), [1] * (number_of - 1)
    while rest > 0:
        candidates = [i for i in range(number_of - 1) if counts[i] < reach]
        mass, budget = sum([loads[i] for i in candidates]), rest
        for i in candidates:
            more = min(reach - counts[i], max(1, budget * loads[i] // mass), rest)
            counts[i] = counts[i] + more
            rest = rest - more
    return np.array([reach] + counts)


def ragged(own_key, number_of, total, reach, skew):
    if number_of == 2:
        one = jax.random.randint(own_key, (), max(1, total - reach), min(reach, total - 1) + 1)
        return jnp.stack([one, total - one])
    lengths = jnp.asarray(length_profile(number_of, total, reach, skew), jnp.int32)
    couples = (number_of - 1) // 2
    source_of, receiver = lengths[1:1 + 2 * couples:2], lengths[2:2 + 2 * couples:2]
    room = jnp.minimum(source_of - 1, reach - receiver)
    shifted = jax.random.randint(jax.random.fold_in(own_key, 1), (couples,), 0, 1 << 20) % (room + 1)
    lengths = lengths.at[1:1 + 2 * couples:2].set(source_of - shifted).at[2:2 + 2 * couples:2].set(receiver + shifted)
    return lengths[jax.random.permutation(jax.random.fold_in(own_key, 2), number_of)]


def centred(key, extent, spread, bound, pieces=(), kind=jnp.bfloat16):
    drawn = jax.random.normal(key, extent, jnp.float32) * spread
    if len(pieces) > 0:
        drawn = block_levels(key, extent, pieces, -0.22, 0.18) * drawn
    return jnp.clip(drawn, min=-bound, max=bound).astype(kind)


def setup_inputs(seed: int = 0) -> dict:
    seeds = jax.random.split(jax.random.key(seed), 6)
    return {
        "affinity_tiles": centred(seeds[0], (TILES, TILE, TILE), 1.0, 6.0, ((0, 256),)),
        "tile_rows": draw_tile_rows(jax.random.fold_in(seeds[5], 71), 0),
        "tile_cols": draw_tile_cols(jax.random.fold_in(seeds[5], 71), 0),
        "lang_counts": ragged(seeds[3], LANGS, DOCS, DOCS // 4, 2).astype(jnp.int32),
        "start_basis": centred(seeds[4], (GRID_COLS, COL_DOCS, VECTORS), 1.0, 6.0, ((0, 8), (1, 32)), jnp.float32),
    }


highest = lax.Precision.HIGHEST

def reference(affinity_tiles, tile_rows, tile_cols, lang_counts, start_basis):
    vectors = start_basis.shape[2]
    basis = start_basis.reshape(DOCS, vectors)
    present = (tile_rows >= 0).astype(jnp.float32)
    row_ids = jnp.clip(tile_rows, 0, BLOCKS - 1).astype(jnp.int32)
    col_ids = jnp.clip(tile_cols, 0, BLOCKS - 1).astype(jnp.int32)
    groups = TILES // TILES_DEV
    group_tiles = affinity_tiles.reshape(groups, TILES_DEV, TILE, TILE)
    group_rows = row_ids.reshape(groups, TILES_DEV)
    group_cols = col_ids.reshape(groups, TILES_DEV)
    group_used = present.reshape(groups, TILES_DEV)

    def degree_step(summed, entries):
        block_set, rows_now, cols_now, weights = entries
        magnitude = jnp.abs(block_set.astype(jnp.float32))
        summed = summed.at[rows_now].add(weights[:, None] * lax.optimization_barrier(jnp.sum(magnitude, axis=2)))
        summed = summed.at[cols_now].add(weights[:, None] * lax.optimization_barrier(jnp.sum(magnitude, axis=1)))
        return (summed, None)
    degree_blocks, _ = lax.scan(degree_step, jnp.zeros((BLOCKS, TILE), jnp.float32), (group_tiles, group_rows, group_cols, group_used))
    degree = 1.0 + degree_blocks.reshape(DOCS)
    inv_root = lax.rsqrt(degree)
    prior_scale = jnp.sum(inv_root) / DOCS
    lang_ends = jnp.cumsum(lang_counts)
    lang_starts = lang_ends - lang_counts
    doc_index = jnp.arange(DOCS, dtype=jnp.int32)
    member = ((doc_index[:, None] >= lang_starts[None, :]) & (doc_index[:, None] < lang_ends[None, :])).astype(jnp.float32)
    counts_real = lang_counts.astype(jnp.float32)
    for iteration in range(ITERS):
        scaled = (inv_root[:, None] * basis).astype(jnp.bfloat16)
        blocks = scaled.reshape(BLOCKS, TILE, vectors)

        def product_step(summed, entries):
            block_set, rows_now, cols_now, weights = entries
            tile_values = block_set.astype(jnp.float32)
            forward = jnp.einsum('tij,tjk->tik', tile_values, blocks[cols_now].astype(jnp.float32), precision=highest)
            backward = jnp.einsum('tij,tik->tjk', tile_values, blocks[rows_now].astype(jnp.float32), precision=highest)
            summed = summed.at[rows_now].add(weights[:, None, None] * forward)
            summed = summed.at[cols_now].add(weights[:, None, None] * backward)
            return (summed, None)
        product_blocks, _ = lax.scan(product_step, jnp.zeros((BLOCKS, TILE, vectors), jnp.float32), (group_tiles, group_rows, group_cols, group_used))
        product = product_blocks.reshape(DOCS, vectors)
        lang_sums = jnp.dot(member.T, basis, precision=highest)
        applied = inv_root[:, None] * product + prior_scale * jnp.dot(member, lang_sums / counts_real[:, None], precision=highest)
        gram_matrix = jnp.dot(applied.T, applied, precision=highest) / DOCS
        factor = jnp.linalg.cholesky(gram_matrix)
        basis = jax.scipy.linalg.solve_triangular(factor, applied.T, lower=True).T
    return basis.reshape(GRID_COLS, COL_DOCS, vectors)
```

```python
import jax
import jax.numpy as jnp
from jax import lax
from jax.sharding import PartitionSpec as P

ROW_BLOCKS = 2
ITERS = 3


highest = lax.Precision.HIGHEST


def membership(first_doc, doc_count, lang_ends, lang_starts):
    doc_index = first_doc + jnp.arange(doc_count, dtype=jnp.int32)
    return (
        (doc_index[:, None] >= lang_starts[None, :]) & (doc_index[:, None] < lang_ends[None, :])
    ).astype(jnp.float32)


def apply_tiles(affinity_tiles, pick_rows, pick_cols, scaled_rows, scaled_cols, col_blocks):
    slot_count, tile_size, _ = affinity_tiles.shape
    vectors = scaled_cols.shape[1]
    blocks_r = scaled_rows.reshape(ROW_BLOCKS, tile_size, vectors)
    blocks_c = scaled_cols.reshape(col_blocks, tile_size, vectors)
    chosen_c = jnp.einsum(
        "tq,qjk->tjk", pick_cols, blocks_c, preferred_element_type=jnp.float32
    ).astype(jnp.bfloat16)
    chosen_r = jnp.einsum(
        "tp,pik->tik", pick_rows, blocks_r, preferred_element_type=jnp.float32
    ).astype(jnp.bfloat16)
    forward = jnp.einsum(
        "tij,tjk->tik", affinity_tiles, chosen_c, preferred_element_type=jnp.float32
    )
    backward = jnp.einsum(
        "tij,tik->tjk", affinity_tiles, chosen_r, preferred_element_type=jnp.float32
    )
    part_rows = jnp.einsum("tp,tik->pik", pick_rows.astype(jnp.float32), forward, precision=highest)
    part_cols = jnp.einsum(
        "tq,tjk->qjk", pick_cols.astype(jnp.float32), backward, precision=highest
    )
    return (
        part_rows.reshape(ROW_BLOCKS * tile_size, vectors),
        part_cols.reshape(col_blocks * tile_size, vectors),
    )


def make_plan(rows, cols):
    group_ratio = rows // cols
    both = ("row", "col")

    def linear(r, c):
        return r * cols + c

    owner_pairs = [
        (linear(r, c), linear((r % group_ratio) * cols + c, r // group_ratio))
        for r in range(rows)
        for c in range(cols)
    ]
    back_pairs = [(dst, src) for src, dst in owner_pairs]

    def to_owner(x):
        return lax.ppermute(x, both, owner_pairs)

    def from_owner(x):
        return lax.ppermute(x, both, back_pairs)

    def halving_scatter(x, axis, size):
        me = lax.axis_index(axis)
        block = x.shape[0] // size
        dist = size // 2
        while dist >= 1:
            upper = (me // dist) % 2
            keep = lax.dynamic_slice_in_dim(x, upper * dist * block, dist * block, 0)
            send = lax.dynamic_slice_in_dim(x, (1 - upper) * dist * block, dist * block, 0)
            pairs = [(i, i ^ dist) for i in range(size)]
            x = keep + lax.ppermute(send, axis, pairs)
            dist //= 2
        return x

    def butterfly_sum(x):
        total = rows * cols
        dist = 1
        while dist < total:
            pairs = [(i, i ^ dist) for i in range(total)]
            x = x + lax.ppermute(x, both, pairs)
            dist *= 2
        return x

    return to_owner, from_owner, halving_scatter, butterfly_sum


def shards(affinity_tiles, tile_rows, tile_cols, lang_counts, start_basis, plan):
    to_owner, from_owner, halving_scatter, butterfly_sum = plan
    row_devices = lax.axis_size("row")
    col_devices = lax.axis_size("col")
    col_blocks = ROW_BLOCKS * row_devices // col_devices
    tile_size = affinity_tiles.shape[1]
    piece_rows = start_basis.shape[1]
    vectors = start_basis.shape[2]
    doc_total = piece_rows * row_devices * col_devices
    my_row = lax.axis_index("row")
    my_col = lax.axis_index("col")
    col_span = col_blocks * tile_size
    piece_offset = my_row * piece_rows
    present = tile_rows >= 0
    local_p = tile_rows - my_row * ROW_BLOCKS
    local_q = tile_cols - my_col * col_blocks
    pick_rows = (
        (local_p[:, None] == jnp.arange(ROW_BLOCKS, dtype=jnp.int32)[None, :]) & present[:, None]
    ).astype(jnp.bfloat16)
    pick_cols = (
        (local_q[:, None] == jnp.arange(col_blocks, dtype=jnp.int32)[None, :]) & present[:, None]
    ).astype(jnp.bfloat16)

    def to_own(rows_part, cols_part):
        from_cols = lax.psum_scatter(cols_part, "row", scatter_dimension=0, tiled=True)
        from_rows = to_owner(halving_scatter(rows_part, "col", col_devices))
        return from_cols + from_rows

    def gather_groups(own):
        cols_all = lax.all_gather(own, "row", axis=0, tiled=True)
        rows_all = lax.all_gather(from_owner(own), "col", axis=0, tiled=True)
        return cols_all, rows_all

    magnitude = jnp.abs(affinity_tiles)
    row_mass = jnp.sum(magnitude, axis=2, dtype=jnp.float32)
    col_mass = jnp.sum(magnitude, axis=1, dtype=jnp.float32)
    degree_rows = jnp.einsum(
        "tp,ti->pi", pick_rows.astype(jnp.float32), row_mass, precision=highest
    ).reshape(ROW_BLOCKS * tile_size, 1)
    degree_cols = jnp.einsum(
        "tq,tj->qj", pick_cols.astype(jnp.float32), col_mass, precision=highest
    ).reshape(col_span, 1)
    inv_own = lax.rsqrt(1.0 + to_own(degree_rows, degree_cols))
    lang_ends = jnp.cumsum(lang_counts)
    lang_starts = lang_ends - lang_counts
    counts_real = lang_counts.astype(jnp.float32)
    member_own = membership(my_col * col_span + piece_offset, piece_rows, lang_ends, lang_starts)
    basis_own = start_basis[0]
    langs = member_own.shape[1]
    first = jnp.concatenate(
        [
            jnp.dot(member_own.T, basis_own, precision=highest),
            jnp.broadcast_to(jnp.sum(inv_own), (1, vectors)),
        ],
        axis=0,
    )
    packed = jnp.concatenate([basis_own, inv_own], axis=1)
    cols_all, rows_all = gather_groups(packed)
    first = butterfly_sum(first)
    lang_now = first[:langs]
    prior_scale = first[langs, 0] / doc_total
    basis_cols, inv_cols = cols_all[:, :vectors], cols_all[:, vectors:]
    basis_rows, inv_rows = rows_all[:, :vectors], rows_all[:, vectors:]
    for iteration in range(ITERS):
        last = iteration == ITERS - 1
        lang_mean = prior_scale * (lang_now / counts_real[:, None])
        scaled_cols = (inv_cols * basis_cols).astype(jnp.bfloat16)
        scaled_rows = (inv_rows * basis_rows).astype(jnp.bfloat16)
        part_rows, part_cols = apply_tiles(
            affinity_tiles, pick_rows, pick_cols, scaled_rows, scaled_cols, col_blocks
        )
        product_own = to_own(part_rows, part_cols)
        applied_own = inv_own * product_own + jnp.dot(member_own, lang_mean, precision=highest)
        gram_part = jnp.dot(applied_own.T, applied_own, precision=highest)
        if last:
            gram_matrix = butterfly_sum(gram_part)
        else:
            lang_part = jnp.dot(member_own.T, applied_own, precision=highest)
            sums = butterfly_sum(jnp.concatenate([gram_part, lang_part], axis=0))
            gram_matrix = sums[:vectors]
            applied_cols, applied_rows = gather_groups(applied_own)
        factor = jnp.linalg.cholesky(gram_matrix / doc_total)
        factor_inv = jax.scipy.linalg.solve_triangular(
            factor, jnp.eye(vectors, dtype=jnp.float32), lower=True
        )
        if last:
            basis_own = jnp.dot(applied_own, factor_inv.T, precision=highest)
        else:
            lang_now = jnp.dot(sums[vectors:], factor_inv.T, precision=highest)
            basis_cols = jnp.dot(applied_cols, factor_inv.T, precision=highest)
            basis_rows = jnp.dot(applied_rows, factor_inv.T, precision=highest)
    return basis_own[None]


def solution(mesh):
    plan = make_plan(mesh.shape["row"], mesh.shape["col"])
    in_specs = (
        P(("row", "col"), None, None),
        P(("row", "col")),
        P(("row", "col")),
        P(),
        P("col", "row", None),
    )
    out_specs = P("col", "row", None)

    def body(*args):
        return shards(*args, plan)

    return jax.shard_map(body, mesh=mesh, in_specs=in_specs, out_specs=out_specs, check_vma=False)
```

```python
import jax
import jax.numpy as jnp
from jax import lax
from jax.sharding import PartitionSpec as P

ROW_BLOCKS = 2
ITERS = 3


highest = lax.Precision.HIGHEST


def membership(first_doc, doc_count, lang_ends, lang_starts):
    doc_index = first_doc + jnp.arange(doc_count, dtype=jnp.int32)
    return (
        (doc_index[:, None] >= lang_starts[None, :]) & (doc_index[:, None] < lang_ends[None, :])
    ).astype(jnp.float32)


def apply_tiles(affinity_tiles, pick_rows, pick_cols, scaled_rows, scaled_cols, col_blocks):
    slot_count, tile_size, _ = affinity_tiles.shape
    vectors = scaled_cols.shape[1]
    blocks_r = scaled_rows.reshape(ROW_BLOCKS, tile_size, vectors)
    blocks_c = scaled_cols.reshape(col_blocks, tile_size, vectors)
    chosen_c = jnp.einsum(
        "tq,qjk->tjk", pick_cols, blocks_c, preferred_element_type=jnp.float32
    ).astype(jnp.bfloat16)
    chosen_r = jnp.einsum(
        "tp,pik->tik", pick_rows, blocks_r, preferred_element_type=jnp.float32
    ).astype(jnp.bfloat16)
    forward = jnp.einsum(
        "tij,tjk->tik", affinity_tiles, chosen_c, preferred_element_type=jnp.float32
    )
    backward = jnp.einsum(
        "tij,tik->tjk", affinity_tiles, chosen_r, preferred_element_type=jnp.float32
    )
    part_rows = jnp.einsum("tp,tik->pik", pick_rows.astype(jnp.float32), forward, precision=highest)
    part_cols = jnp.einsum(
        "tq,tjk->qjk", pick_cols.astype(jnp.float32), backward, precision=highest
    )
    return (
        part_rows.reshape(ROW_BLOCKS * tile_size, vectors),
        part_cols.reshape(col_blocks * tile_size, vectors),
    )


def make_plan(rows, cols):
    group_ratio = rows // cols
    both = ("row", "col")

    def linear(r, c):
        return r * cols + c

    owner_pairs = [
        (linear(r, c), linear((r % group_ratio) * cols + c, r // group_ratio))
        for r in range(rows)
        for c in range(cols)
    ]
    back_pairs = [(dst, src) for src, dst in owner_pairs]

    def to_owner(x):
        return lax.ppermute(x, both, owner_pairs)

    def from_owner(x):
        return lax.ppermute(x, both, back_pairs)

    def halving_scatter(x, axis, size):
        me = lax.axis_index(axis)
        bits = size.bit_length() - 1
        block = x.shape[0] // size
        rest = x.shape[1:]
        x = x.reshape((2,) * bits + (block,) + rest)
        for bit in range(bits):
            place = bits - 1 - bit
            mine = (me >> bit) & 1
            keep = lax.dynamic_index_in_dim(x, mine, axis=place, keepdims=False)
            send = lax.dynamic_index_in_dim(x, 1 - mine, axis=place, keepdims=False)
            pairs = [(i, i ^ (1 << bit)) for i in range(size)]
            x = keep + lax.ppermute(send, axis, pairs)
        return x.reshape((block,) + rest)

    def doubling_gather(x, axis, size):
        me = lax.axis_index(axis)
        bits = size.bit_length() - 1
        block = x.shape[0]
        rest = x.shape[1:]
        for step in range(bits):
            bit = bits - 1 - step
            upper = ((me >> bit) & 1) == 1
            pairs = [(i, i ^ (1 << bit)) for i in range(size)]
            other = lax.ppermute(x, axis, pairs)
            low = jnp.where(upper, other, x)
            high = jnp.where(upper, x, other)
            x = jnp.stack([low, high], axis=step)
        return x.reshape((size * block,) + rest)

    def butterfly_sum(x):
        total = rows * cols
        dist = 1
        while dist < total:
            pairs = [(i, i ^ dist) for i in range(total)]
            x = x + lax.ppermute(x, both, pairs)
            dist *= 2
        return x

    return to_owner, from_owner, halving_scatter, doubling_gather, butterfly_sum


def shards(affinity_tiles, tile_rows, tile_cols, lang_counts, start_basis, plan):
    to_owner, from_owner, halving_scatter, doubling_gather, butterfly_sum = plan
    row_devices = lax.axis_size("row")
    col_devices = lax.axis_size("col")
    col_blocks = ROW_BLOCKS * row_devices // col_devices
    tile_size = affinity_tiles.shape[1]
    piece_rows = start_basis.shape[1]
    vectors = start_basis.shape[2]
    doc_total = piece_rows * row_devices * col_devices
    my_row = lax.axis_index("row")
    my_col = lax.axis_index("col")
    col_span = col_blocks * tile_size
    piece_offset = my_row * piece_rows
    present = tile_rows >= 0
    local_p = tile_rows - my_row * ROW_BLOCKS
    local_q = tile_cols - my_col * col_blocks
    pick_rows = (
        (local_p[:, None] == jnp.arange(ROW_BLOCKS, dtype=jnp.int32)[None, :]) & present[:, None]
    ).astype(jnp.bfloat16)
    pick_cols = (
        (local_q[:, None] == jnp.arange(col_blocks, dtype=jnp.int32)[None, :]) & present[:, None]
    ).astype(jnp.bfloat16)

    def to_own(rows_part, cols_part):
        from_cols = halving_scatter(cols_part, "row", row_devices)
        from_rows = to_owner(halving_scatter(rows_part, "col", col_devices))
        return from_cols + from_rows

    def gather_groups(own):
        cols_all = doubling_gather(own, "row", row_devices)
        rows_all = doubling_gather(from_owner(own), "col", col_devices)
        return cols_all, rows_all

    magnitude = jnp.abs(affinity_tiles)
    row_mass = jnp.sum(magnitude, axis=2, dtype=jnp.float32)
    col_mass = jnp.sum(magnitude, axis=1, dtype=jnp.float32)
    degree_rows = jnp.einsum(
        "tp,ti->pi", pick_rows.astype(jnp.float32), row_mass, precision=highest
    ).reshape(ROW_BLOCKS * tile_size, 1)
    degree_cols = jnp.einsum(
        "tq,tj->qj", pick_cols.astype(jnp.float32), col_mass, precision=highest
    ).reshape(col_span, 1)
    inv_own = lax.rsqrt(1.0 + to_own(degree_rows, degree_cols))
    lang_ends = jnp.cumsum(lang_counts)
    lang_starts = lang_ends - lang_counts
    counts_real = lang_counts.astype(jnp.float32)
    member_own = membership(my_col * col_span + piece_offset, piece_rows, lang_ends, lang_starts)
    basis_own = start_basis[0]
    langs = member_own.shape[1]
    first = jnp.concatenate(
        [
            jnp.dot(member_own.T, basis_own, precision=highest),
            jnp.broadcast_to(jnp.sum(inv_own), (1, vectors)),
        ],
        axis=0,
    )
    packed = jnp.concatenate([basis_own, inv_own], axis=1)
    cols_all, rows_all = gather_groups(packed)
    first = butterfly_sum(first)
    lang_now = first[:langs]
    prior_scale = first[langs, 0] / doc_total
    basis_cols, inv_cols = cols_all[:, :vectors], cols_all[:, vectors:]
    basis_rows, inv_rows = rows_all[:, :vectors], rows_all[:, vectors:]
    for iteration in range(ITERS):
        last = iteration == ITERS - 1
        lang_mean = prior_scale * (lang_now / counts_real[:, None])
        scaled_cols = (inv_cols * basis_cols).astype(jnp.bfloat16)
        scaled_rows = (inv_rows * basis_rows).astype(jnp.bfloat16)
        part_rows, part_cols = apply_tiles(
            affinity_tiles, pick_rows, pick_cols, scaled_rows, scaled_cols, col_blocks
        )
        product_own = to_own(part_rows, part_cols)
        applied_own = inv_own * product_own + jnp.dot(member_own, lang_mean, precision=highest)
        gram_part = jnp.dot(applied_own.T, applied_own, precision=highest)
        if last:
            gram_matrix = butterfly_sum(gram_part)
        else:
            lang_part = jnp.dot(member_own.T, applied_own, precision=highest)
            sums = butterfly_sum(jnp.concatenate([gram_part, lang_part], axis=0))
            gram_matrix = sums[:vectors]
            applied_cols, applied_rows = gather_groups(applied_own)
        factor = jnp.linalg.cholesky(gram_matrix / doc_total)
        factor_inv = jax.scipy.linalg.solve_triangular(
            factor, jnp.eye(vectors, dtype=jnp.float32), lower=True
        )
        if last:
            basis_own = jnp.dot(applied_own, factor_inv.T, precision=highest)
        else:
            lang_now = jnp.dot(sums[vectors:], factor_inv.T, precision=highest)
            basis_cols = jnp.dot(applied_cols, factor_inv.T, precision=highest)
            basis_rows = jnp.dot(applied_rows, factor_inv.T, precision=highest)
    return basis_own[None]


def solution(mesh):
    plan = make_plan(mesh.shape["row"], mesh.shape["col"])
    in_specs = (
        P(("row", "col"), None, None),
        P(("row", "col")),
        P(("row", "col")),
        P(),
        P("col", "row", None),
    )
    out_specs = P("col", "row", None)

    def body(*args):
        return shards(*args, plan)

    return jax.shard_map(body, mesh=mesh, in_specs=in_specs, out_specs=out_specs, check_vma=False)
```

```python
import jax
import jax.numpy as jnp
from jax import lax
from jax.sharding import PartitionSpec as P

ROW_BLOCKS = 2
ITERS = 3


highest = lax.Precision.HIGHEST


def membership(first_doc, doc_count, lang_ends, lang_starts):
    doc_index = first_doc + jnp.arange(doc_count, dtype=jnp.int32)
    return (
        (doc_index[:, None] >= lang_starts[None, :]) & (doc_index[:, None] < lang_ends[None, :])
    ).astype(jnp.float32)


def apply_tiles(affinity_tiles, pick_rows, pick_cols, scaled_rows, scaled_cols, col_blocks):
    slot_count, tile_size, _ = affinity_tiles.shape
    vectors = scaled_cols.shape[1]
    blocks_r = scaled_rows.reshape(ROW_BLOCKS, tile_size, vectors)
    blocks_c = scaled_cols.reshape(col_blocks, tile_size, vectors)
    chosen_c = jnp.einsum(
        "tq,qjk->tjk", pick_cols, blocks_c, preferred_element_type=jnp.float32
    ).astype(jnp.bfloat16)
    chosen_r = jnp.einsum(
        "tp,pik->tik", pick_rows, blocks_r, preferred_element_type=jnp.float32
    ).astype(jnp.bfloat16)
    forward = jnp.einsum(
        "tij,tjk->tik", affinity_tiles, chosen_c, preferred_element_type=jnp.float32
    )
    backward = jnp.einsum(
        "tij,tik->tjk", affinity_tiles, chosen_r, preferred_element_type=jnp.float32
    )
    part_rows = jnp.einsum("tp,tik->pik", pick_rows.astype(jnp.float32), forward, precision=highest)
    part_cols = jnp.einsum(
        "tq,tjk->qjk", pick_cols.astype(jnp.float32), backward, precision=highest
    )
    return (
        part_rows.reshape(ROW_BLOCKS * tile_size, vectors),
        part_cols.reshape(col_blocks * tile_size, vectors),
    )


def make_plan(rows, cols):
    group_ratio = rows // cols
    both = ("row", "col")

    def linear(r, c):
        return r * cols + c

    owner_pairs = [
        (linear(r, c), linear((r % group_ratio) * cols + c, r // group_ratio))
        for r in range(rows)
        for c in range(cols)
    ]
    back_pairs = [(dst, src) for src, dst in owner_pairs]

    def to_owner(x):
        return lax.ppermute(x, both, owner_pairs)

    def from_owner(x):
        return lax.ppermute(x, both, back_pairs)

    def halving_scatter(x, axis, size):
        me = lax.axis_index(axis)
        bits = size.bit_length() - 1
        block = x.shape[0] // size
        rest = x.shape[1:]
        x = x.reshape((2,) * bits + (block,) + rest)
        for bit in range(bits):
            place = bits - 1 - bit
            mine = (me >> bit) & 1
            keep = lax.dynamic_index_in_dim(x, mine, axis=place, keepdims=False)
            send = lax.dynamic_index_in_dim(x, 1 - mine, axis=place, keepdims=False)
            pairs = [(i, i ^ (1 << bit)) for i in range(size)]
            x = keep + lax.ppermute(send, axis, pairs)
        return x.reshape((block,) + rest)

    def doubling_gather(x, axis, size):
        me = lax.axis_index(axis)
        bits = size.bit_length() - 1
        block = x.shape[0]
        rest = x.shape[1:]
        for step in range(bits):
            bit = bits - 1 - step
            upper = ((me >> bit) & 1) == 1
            pairs = [(i, i ^ (1 << bit)) for i in range(size)]
            other = lax.ppermute(x, axis, pairs)
            low = jnp.where(upper, other, x)
            high = jnp.where(upper, x, other)
            x = jnp.stack([low, high], axis=step)
        return x.reshape((size * block,) + rest)

    def butterfly_sum(x):
        total = rows * cols
        me = lax.axis_index("row") * cols + lax.axis_index("col")
        shift = 0
        while (1 << shift) < total:
            if (4 << shift) <= total:
                digit = (me >> shift) % 4
                got = [x]
                for step in (1, 2, 3):
                    pairs = []
                    for i in range(total):
                        d = (i >> shift) % 4
                        j = i - (d << shift) + (((d - step) % 4) << shift)
                        pairs.append((i, j))
                    got.append(lax.ppermute(x, both, pairs))
                stacked = jnp.stack(got)
                by_digit = [
                    lax.dynamic_index_in_dim(stacked, (k - digit) % 4, 0, keepdims=False)
                    for k in range(4)
                ]
                x = (by_digit[0] + by_digit[1]) + (by_digit[2] + by_digit[3])
                shift += 2
            else:
                pairs = [(i, i ^ (1 << shift)) for i in range(total)]
                x = x + lax.ppermute(x, both, pairs)
                shift += 1
        return x

    return to_owner, from_owner, halving_scatter, doubling_gather, butterfly_sum


def shards(affinity_tiles, tile_rows, tile_cols, lang_counts, start_basis, plan):
    to_owner, from_owner, halving_scatter, doubling_gather, butterfly_sum = plan
    row_devices = lax.axis_size("row")
    col_devices = lax.axis_size("col")
    col_blocks = ROW_BLOCKS * row_devices // col_devices
    tile_size = affinity_tiles.shape[1]
    piece_rows = start_basis.shape[1]
    vectors = start_basis.shape[2]
    doc_total = piece_rows * row_devices * col_devices
    my_row = lax.axis_index("row")
    my_col = lax.axis_index("col")
    col_span = col_blocks * tile_size
    piece_offset = my_row * piece_rows
    present = tile_rows >= 0
    local_p = tile_rows - my_row * ROW_BLOCKS
    local_q = tile_cols - my_col * col_blocks
    pick_rows = (
        (local_p[:, None] == jnp.arange(ROW_BLOCKS, dtype=jnp.int32)[None, :]) & present[:, None]
    ).astype(jnp.bfloat16)
    pick_cols = (
        (local_q[:, None] == jnp.arange(col_blocks, dtype=jnp.int32)[None, :]) & present[:, None]
    ).astype(jnp.bfloat16)

    def to_own(rows_part, cols_part):
        from_cols = halving_scatter(cols_part, "row", row_devices)
        from_rows = to_owner(halving_scatter(rows_part, "col", col_devices))
        return from_cols + from_rows

    def gather_groups(own):
        cols_all = doubling_gather(own, "row", row_devices)
        rows_all = doubling_gather(from_owner(own), "col", col_devices)
        return cols_all, rows_all

    magnitude = jnp.abs(affinity_tiles)
    row_mass = jnp.sum(magnitude, axis=2, dtype=jnp.float32)
    col_mass = jnp.sum(magnitude, axis=1, dtype=jnp.float32)
    degree_rows = jnp.einsum(
        "tp,ti->pi", pick_rows.astype(jnp.float32), row_mass, precision=highest
    ).reshape(ROW_BLOCKS * tile_size, 1)
    degree_cols = jnp.einsum(
        "tq,tj->qj", pick_cols.astype(jnp.float32), col_mass, precision=highest
    ).reshape(col_span, 1)
    inv_own = lax.rsqrt(1.0 + to_own(degree_rows, degree_cols))
    lang_ends = jnp.cumsum(lang_counts)
    lang_starts = lang_ends - lang_counts
    counts_real = lang_counts.astype(jnp.float32)
    member_own = membership(my_col * col_span + piece_offset, piece_rows, lang_ends, lang_starts)
    basis_own = start_basis[0]
    langs = member_own.shape[1]
    first = jnp.concatenate(
        [
            jnp.dot(member_own.T, basis_own, precision=highest),
            jnp.broadcast_to(jnp.sum(inv_own), (1, vectors)),
        ],
        axis=0,
    )
    packed = jnp.concatenate([basis_own, inv_own], axis=1)
    cols_all, rows_all = gather_groups(packed)
    first = butterfly_sum(first)
    lang_now = first[:langs]
    prior_scale = first[langs, 0] / doc_total
    basis_cols, inv_cols = cols_all[:, :vectors], cols_all[:, vectors:]
    basis_rows, inv_rows = rows_all[:, :vectors], rows_all[:, vectors:]
    for iteration in range(ITERS):
        last = iteration == ITERS - 1
        lang_mean = prior_scale * (lang_now / counts_real[:, None])
        scaled_cols = (inv_cols * basis_cols).astype(jnp.bfloat16)
        scaled_rows = (inv_rows * basis_rows).astype(jnp.bfloat16)
        part_rows, part_cols = apply_tiles(
            affinity_tiles, pick_rows, pick_cols, scaled_rows, scaled_cols, col_blocks
        )
        product_own = to_own(part_rows, part_cols)
        applied_own = inv_own * product_own + jnp.dot(member_own, lang_mean, precision=highest)
        gram_part = jnp.dot(applied_own.T, applied_own, precision=highest)
        if last:
            gram_matrix = butterfly_sum(gram_part)
        else:
            lang_part = jnp.dot(member_own.T, applied_own, precision=highest)
            sums = butterfly_sum(jnp.concatenate([gram_part, lang_part], axis=0))
            gram_matrix = sums[:vectors]
            applied_cols, applied_rows = gather_groups(applied_own)
        factor = jnp.linalg.cholesky(gram_matrix / doc_total)
        factor_inv = jax.scipy.linalg.solve_triangular(
            factor, jnp.eye(vectors, dtype=jnp.float32), lower=True
        )
        if last:
            basis_own = jnp.dot(applied_own, factor_inv.T, precision=highest)
        else:
            lang_now = jnp.dot(sums[vectors:], factor_inv.T, precision=highest)
            basis_cols = jnp.dot(applied_cols, factor_inv.T, precision=highest)
            basis_rows = jnp.dot(applied_rows, factor_inv.T, precision=highest)
    return basis_own[None]


def solution(mesh):
    plan = make_plan(mesh.shape["row"], mesh.shape["col"])
    in_specs = (
        P(("row", "col"), None, None),
        P(("row", "col")),
        P(("row", "col")),
        P(),
        P("col", "row", None),
    )
    out_specs = P("col", "row", None)

    def body(*args):
        return shards(*args, plan)

    return jax.shard_map(body, mesh=mesh, in_specs=in_specs, out_specs=out_specs, check_vma=False)
```

```python
import jax
import jax.numpy as jnp
from jax import lax
from jax.sharding import PartitionSpec as P

ROW_BLOCKS = 2
ITERS = 3


highest = lax.Precision.HIGHEST


def membership(first_doc, doc_count, lang_ends, lang_starts):
    doc_index = first_doc + jnp.arange(doc_count, dtype=jnp.int32)
    return (
        (doc_index[:, None] >= lang_starts[None, :]) & (doc_index[:, None] < lang_ends[None, :])
    ).astype(jnp.float32)


def apply_tiles(affinity_tiles, pick_rows, pick_cols, scaled_rows, scaled_cols, col_blocks):
    slot_count, tile_size, _ = affinity_tiles.shape
    vectors = scaled_cols.shape[1]
    blocks_r = scaled_rows.reshape(ROW_BLOCKS, tile_size, vectors)
    blocks_c = scaled_cols.reshape(col_blocks, tile_size, vectors)
    chosen_c = jnp.einsum(
        "tq,qjk->tjk", pick_cols, blocks_c, preferred_element_type=jnp.float32
    ).astype(jnp.bfloat16)
    chosen_r = jnp.einsum(
        "tp,pik->tik", pick_rows, blocks_r, preferred_element_type=jnp.float32
    ).astype(jnp.bfloat16)
    forward = jnp.einsum(
        "tij,tjk->tik", affinity_tiles, chosen_c, preferred_element_type=jnp.float32
    )
    backward = jnp.einsum(
        "tij,tik->tjk", affinity_tiles, chosen_r, preferred_element_type=jnp.float32
    )
    part_rows = jnp.einsum("tp,tik->pik", pick_rows.astype(jnp.float32), forward, precision=highest)
    part_cols = jnp.einsum(
        "tq,tjk->qjk", pick_cols.astype(jnp.float32), backward, precision=highest
    )
    return (
        part_rows.reshape(ROW_BLOCKS * tile_size, vectors),
        part_cols.reshape(col_blocks * tile_size, vectors),
    )


def make_plan(rows, cols):
    group_ratio = rows // cols
    both = ("row", "col")

    def linear(r, c):
        return r * cols + c

    owner_pairs = [
        (linear(r, c), linear((r % group_ratio) * cols + c, r // group_ratio))
        for r in range(rows)
        for c in range(cols)
    ]
    back_pairs = [(dst, src) for src, dst in owner_pairs]

    def to_owner(x):
        return lax.ppermute(x, both, owner_pairs)

    def from_owner(x):
        return lax.ppermute(x, both, back_pairs)

    def digits(size):
        out, shift = [], 0
        while (1 << shift) < size:
            radix = 4 if (4 << shift) <= size else 2
            out.append((shift, radix))
            shift += radix.bit_length() - 1
        return out

    def shifted_pairs(size, shift, radix, step):
        pairs = []
        for i in range(size):
            e = (i >> shift) % radix
            pairs.append((i, i - (e << shift) + (((e - step) % radix) << shift)))
        return pairs

    def halving_scatter(x, axis, size):
        me = lax.axis_index(axis)
        places = digits(size)
        block = x.shape[0] // size
        rest = x.shape[1:]
        x = x.reshape(tuple(radix for _, radix in reversed(places)) + (block,) + rest)
        for j, (shift, radix) in enumerate(places):
            place = len(places) - 1 - j
            mine = (me >> shift) % radix
            total = lax.dynamic_index_in_dim(x, mine, axis=place, keepdims=False)
            for step in range(1, radix):
                send = lax.dynamic_index_in_dim(x, (mine - step) % radix, axis=place, keepdims=False)
                total = total + lax.ppermute(send, axis, shifted_pairs(size, shift, radix, step))
            x = total
        return x.reshape((block,) + rest)

    def doubling_gather(x, axis, size):
        me = lax.axis_index(axis)
        block = x.shape[0]
        rest = x.shape[1:]
        for step_no, (shift, radix) in enumerate(reversed(digits(size))):
            mine = (me >> shift) % radix
            got = [x]
            for step in range(1, radix):
                got.append(lax.ppermute(x, axis, shifted_pairs(size, shift, radix, step)))
            stacked = jnp.stack(got)
            by_digit = [
                lax.dynamic_index_in_dim(stacked, (k - mine) % radix, 0, keepdims=False)
                for k in range(radix)
            ]
            x = jnp.stack(by_digit, axis=step_no)
        return x.reshape((size * block,) + rest)

    def butterfly_sum(x):
        total = rows * cols
        me = lax.axis_index("row") * cols + lax.axis_index("col")
        shift = 0
        while (1 << shift) < total:
            if (4 << shift) <= total:
                digit = (me >> shift) % 4
                got = [x]
                for step in (1, 2, 3):
                    pairs = []
                    for i in range(total):
                        d = (i >> shift) % 4
                        j = i - (d << shift) + (((d - step) % 4) << shift)
                        pairs.append((i, j))
                    got.append(lax.ppermute(x, both, pairs))
                stacked = jnp.stack(got)
                by_digit = [
                    lax.dynamic_index_in_dim(stacked, (k - digit) % 4, 0, keepdims=False)
                    for k in range(4)
                ]
                x = (by_digit[0] + by_digit[1]) + (by_digit[2] + by_digit[3])
                shift += 2
            else:
                pairs = [(i, i ^ (1 << shift)) for i in range(total)]
                x = x + lax.ppermute(x, both, pairs)
                shift += 1
        return x

    return to_owner, from_owner, halving_scatter, doubling_gather, butterfly_sum


def shards(affinity_tiles, tile_rows, tile_cols, lang_counts, start_basis, plan):
    to_owner, from_owner, halving_scatter, doubling_gather, butterfly_sum = plan
    row_devices = lax.axis_size("row")
    col_devices = lax.axis_size("col")
    col_blocks = ROW_BLOCKS * row_devices // col_devices
    tile_size = affinity_tiles.shape[1]
    piece_rows = start_basis.shape[1]
    vectors = start_basis.shape[2]
    doc_total = piece_rows * row_devices * col_devices
    my_row = lax.axis_index("row")
    my_col = lax.axis_index("col")
    col_span = col_blocks * tile_size
    piece_offset = my_row * piece_rows
    present = tile_rows >= 0
    local_p = tile_rows - my_row * ROW_BLOCKS
    local_q = tile_cols - my_col * col_blocks
    pick_rows = (
        (local_p[:, None] == jnp.arange(ROW_BLOCKS, dtype=jnp.int32)[None, :]) & present[:, None]
    ).astype(jnp.bfloat16)
    pick_cols = (
        (local_q[:, None] == jnp.arange(col_blocks, dtype=jnp.int32)[None, :]) & present[:, None]
    ).astype(jnp.bfloat16)

    def to_own(rows_part, cols_part):
        from_cols = halving_scatter(cols_part, "row", row_devices)
        from_rows = to_owner(halving_scatter(rows_part, "col", col_devices))
        return from_cols + from_rows

    def gather_groups(own):
        cols_all = doubling_gather(own, "row", row_devices)
        rows_all = doubling_gather(from_owner(own), "col", col_devices)
        return cols_all, rows_all

    magnitude = jnp.abs(affinity_tiles)
    row_mass = jnp.sum(magnitude, axis=2, dtype=jnp.float32)
    col_mass = jnp.sum(magnitude, axis=1, dtype=jnp.float32)
    degree_rows = jnp.einsum(
        "tp,ti->pi", pick_rows.astype(jnp.float32), row_mass, precision=highest
    ).reshape(ROW_BLOCKS * tile_size, 1)
    degree_cols = jnp.einsum(
        "tq,tj->qj", pick_cols.astype(jnp.float32), col_mass, precision=highest
    ).reshape(col_span, 1)
    inv_own = lax.rsqrt(1.0 + to_own(degree_rows, degree_cols))
    lang_ends = jnp.cumsum(lang_counts)
    lang_starts = lang_ends - lang_counts
    counts_real = lang_counts.astype(jnp.float32)
    member_own = membership(my_col * col_span + piece_offset, piece_rows, lang_ends, lang_starts)
    basis_own = start_basis[0]
    langs = member_own.shape[1]
    first = jnp.concatenate(
        [
            jnp.dot(member_own.T, basis_own, precision=highest),
            jnp.broadcast_to(jnp.sum(inv_own), (1, vectors)),
        ],
        axis=0,
    )
    packed = jnp.concatenate([basis_own, inv_own], axis=1)
    cols_all, rows_all = gather_groups(packed)
    first = butterfly_sum(first)
    lang_now = first[:langs]
    prior_scale = first[langs, 0] / doc_total
    basis_cols, inv_cols = cols_all[:, :vectors], cols_all[:, vectors:]
    basis_rows, inv_rows = rows_all[:, :vectors], rows_all[:, vectors:]
    for iteration in range(ITERS):
        last = iteration == ITERS - 1
        lang_mean = prior_scale * (lang_now / counts_real[:, None])
        scaled_cols = (inv_cols * basis_cols).astype(jnp.bfloat16)
        scaled_rows = (inv_rows * basis_rows).astype(jnp.bfloat16)
        part_rows, part_cols = apply_tiles(
            affinity_tiles, pick_rows, pick_cols, scaled_rows, scaled_cols, col_blocks
        )
        product_own = to_own(part_rows, part_cols)
        applied_own = inv_own * product_own + jnp.dot(member_own, lang_mean, precision=highest)
        gram_part = jnp.dot(applied_own.T, applied_own, precision=highest)
        if last:
            gram_matrix = butterfly_sum(gram_part)
        else:
            lang_part = jnp.dot(member_own.T, applied_own, precision=highest)
            sums = butterfly_sum(jnp.concatenate([gram_part, lang_part], axis=0))
            gram_matrix = sums[:vectors]
            applied_cols, applied_rows = gather_groups(applied_own)
        factor = jnp.linalg.cholesky(gram_matrix / doc_total)
        factor_inv = jax.scipy.linalg.solve_triangular(
            factor, jnp.eye(vectors, dtype=jnp.float32), lower=True
        )
        if last:
            basis_own = jnp.dot(applied_own, factor_inv.T, precision=highest)
        else:
            lang_now = jnp.dot(sums[vectors:], factor_inv.T, precision=highest)
            basis_cols = jnp.dot(applied_cols, factor_inv.T, precision=highest)
            basis_rows = jnp.dot(applied_rows, factor_inv.T, precision=highest)
    return basis_own[None]


def solution(mesh):
    plan = make_plan(mesh.shape["row"], mesh.shape["col"])
    in_specs = (
        P(("row", "col"), None, None),
        P(("row", "col")),
        P(("row", "col")),
        P(),
        P("col", "row", None),
    )
    out_specs = P("col", "row", None)

    def body(*args):
        return shards(*args, plan)

    return jax.shard_map(body, mesh=mesh, in_specs=in_specs, out_specs=out_specs, check_vma=False)
```

```python
import jax
import jax.numpy as jnp
from jax import lax
from jax.sharding import PartitionSpec as P

ROW_BLOCKS = 2
ITERS = 3


highest = lax.Precision.HIGHEST


def membership(first_doc, doc_count, lang_ends, lang_starts):
    doc_index = first_doc + jnp.arange(doc_count, dtype=jnp.int32)
    return (
        (doc_index[:, None] >= lang_starts[None, :]) & (doc_index[:, None] < lang_ends[None, :])
    ).astype(jnp.float32)


def apply_tiles(affinity_tiles, pick_rows, pick_cols, scaled_rows, scaled_cols, col_blocks):
    slot_count, tile_size, _ = affinity_tiles.shape
    vectors = scaled_cols.shape[1]
    blocks_r = scaled_rows.reshape(ROW_BLOCKS, tile_size, vectors)
    blocks_c = scaled_cols.reshape(col_blocks, tile_size, vectors)
    chosen_c = jnp.einsum(
        "tq,qjk->tjk", pick_cols, blocks_c, preferred_element_type=jnp.float32
    ).astype(jnp.bfloat16)
    chosen_r = jnp.einsum(
        "tp,pik->tik", pick_rows, blocks_r, preferred_element_type=jnp.float32
    ).astype(jnp.bfloat16)
    forward = jnp.einsum(
        "tij,tjk->tik", affinity_tiles, chosen_c, preferred_element_type=jnp.float32
    )
    backward = jnp.einsum(
        "tij,tik->tjk", affinity_tiles, chosen_r, preferred_element_type=jnp.float32
    )
    part_rows = jnp.einsum("tp,tik->pik", pick_rows.astype(jnp.float32), forward, precision=highest)
    part_cols = jnp.einsum(
        "tq,tjk->qjk", pick_cols.astype(jnp.float32), backward, precision=highest
    )
    return (
        part_rows.reshape(ROW_BLOCKS * tile_size, vectors),
        part_cols.reshape(col_blocks * tile_size, vectors),
    )


def make_plan(rows, cols):
    group_ratio = rows // cols
    both = ("row", "col")

    def linear(r, c):
        return r * cols + c

    owner_pairs = [
        (linear(r, c), linear((r % group_ratio) * cols + c, r // group_ratio))
        for r in range(rows)
        for c in range(cols)
    ]
    back_pairs = [(dst, src) for src, dst in owner_pairs]

    def to_owner(x):
        return lax.ppermute(x, both, owner_pairs)

    def from_owner(x):
        return lax.ppermute(x, both, back_pairs)

    def halving_scatter(x, axis, size):
        me = lax.axis_index(axis)
        bits = size.bit_length() - 1
        block = x.shape[0] // size
        rest = x.shape[1:]
        x = x.reshape((2,) * bits + (block,) + rest)
        for bit in range(bits):
            place = bits - 1 - bit
            mine = (me >> bit) & 1
            keep = lax.dynamic_index_in_dim(x, mine, axis=place, keepdims=False)
            send = lax.dynamic_index_in_dim(x, 1 - mine, axis=place, keepdims=False)
            pairs = [(i, i ^ (1 << bit)) for i in range(size)]
            x = keep + lax.ppermute(send, axis, pairs)
        return x.reshape((block,) + rest)

    def doubling_gather(x, axis, size):
        me = lax.axis_index(axis)
        bits = size.bit_length() - 1
        block = x.shape[0]
        rest = x.shape[1:]
        for step in range(bits):
            bit = bits - 1 - step
            upper = ((me >> bit) & 1) == 1
            pairs = [(i, i ^ (1 << bit)) for i in range(size)]
            other = lax.ppermute(x, axis, pairs)
            low = jnp.where(upper, other, x)
            high = jnp.where(upper, x, other)
            x = jnp.stack([low, high], axis=step)
        return x.reshape((size * block,) + rest)

    def gather_with_sum(x, axis, size, small):
        me = lax.axis_index(axis)
        bits = size.bit_length() - 1
        block = x.shape[0]
        rest = x.shape[1:]
        for step in range(bits):
            bit = bits - 1 - step
            upper = ((me >> bit) & 1) == 1
            pairs = [(i, i ^ (1 << bit)) for i in range(size)]
            width = x.shape[-1]
            flat = x.reshape(-1, width)
            rows_x = flat.shape[0]
            extra = jnp.pad(small, ((0, 0), (0, width - small.shape[1])))
            got = lax.ppermute(jnp.concatenate([flat, extra], axis=0), axis, pairs)
            other = got[:rows_x].reshape(x.shape)
            other_small = got[rows_x:, : small.shape[1]]
            small = small + other_small
            low = jnp.where(upper, other, x)
            high = jnp.where(upper, x, other)
            x = jnp.stack([low, high], axis=step)
        return x.reshape((size * block,) + rest), small

    def butterfly_sum(x):
        total = rows * cols
        me = lax.axis_index("row") * cols + lax.axis_index("col")
        shift = 0
        while (1 << shift) < total:
            if (4 << shift) <= total:
                digit = (me >> shift) % 4
                got = [x]
                for step in (1, 2, 3):
                    pairs = []
                    for i in range(total):
                        d = (i >> shift) % 4
                        j = i - (d << shift) + (((d - step) % 4) << shift)
                        pairs.append((i, j))
                    got.append(lax.ppermute(x, both, pairs))
                stacked = jnp.stack(got)
                by_digit = [
                    lax.dynamic_index_in_dim(stacked, (k - digit) % 4, 0, keepdims=False)
                    for k in range(4)
                ]
                x = (by_digit[0] + by_digit[1]) + (by_digit[2] + by_digit[3])
                shift += 2
            else:
                pairs = [(i, i ^ (1 << shift)) for i in range(total)]
                x = x + lax.ppermute(x, both, pairs)
                shift += 1
        return x

    return to_owner, from_owner, halving_scatter, gather_with_sum, butterfly_sum


def shards(affinity_tiles, tile_rows, tile_cols, lang_counts, start_basis, plan):
    to_owner, from_owner, halving_scatter, gather_with_sum, butterfly_sum = plan
    row_devices = lax.axis_size("row")
    col_devices = lax.axis_size("col")
    col_blocks = ROW_BLOCKS * row_devices // col_devices
    tile_size = affinity_tiles.shape[1]
    piece_rows = start_basis.shape[1]
    vectors = start_basis.shape[2]
    doc_total = piece_rows * row_devices * col_devices
    my_row = lax.axis_index("row")
    my_col = lax.axis_index("col")
    col_span = col_blocks * tile_size
    piece_offset = my_row * piece_rows
    present = tile_rows >= 0
    local_p = tile_rows - my_row * ROW_BLOCKS
    local_q = tile_cols - my_col * col_blocks
    pick_rows = (
        (local_p[:, None] == jnp.arange(ROW_BLOCKS, dtype=jnp.int32)[None, :]) & present[:, None]
    ).astype(jnp.bfloat16)
    pick_cols = (
        (local_q[:, None] == jnp.arange(col_blocks, dtype=jnp.int32)[None, :]) & present[:, None]
    ).astype(jnp.bfloat16)

    def to_own(rows_part, cols_part):
        from_cols = halving_scatter(cols_part, "row", row_devices)
        from_rows = to_owner(halving_scatter(rows_part, "col", col_devices))
        return from_cols + from_rows

    def gather_groups(own, small):
        seed = from_owner(own)
        cols_all, small = gather_with_sum(own, "row", row_devices, small)
        rows_all, small = gather_with_sum(seed, "col", col_devices, small)
        return cols_all, rows_all, small

    magnitude = jnp.abs(affinity_tiles)
    row_mass = jnp.sum(magnitude, axis=2, dtype=jnp.float32)
    col_mass = jnp.sum(magnitude, axis=1, dtype=jnp.float32)
    degree_rows = jnp.einsum(
        "tp,ti->pi", pick_rows.astype(jnp.float32), row_mass, precision=highest
    ).reshape(col_devices, piece_rows)
    degree_cols = jnp.einsum(
        "tq,tj->qj", pick_cols.astype(jnp.float32), col_mass, precision=highest
    ).reshape(row_devices, piece_rows)
    inv_own = lax.rsqrt(1.0 + to_own(degree_rows, degree_cols)).reshape(piece_rows, 1)
    lang_ends = jnp.cumsum(lang_counts)
    lang_starts = lang_ends - lang_counts
    counts_real = lang_counts.astype(jnp.float32)
    member_own = membership(my_col * col_span + piece_offset, piece_rows, lang_ends, lang_starts)
    basis_own = start_basis[0]
    langs = member_own.shape[1]
    first = jnp.concatenate(
        [
            jnp.dot(member_own.T, basis_own, precision=highest),
            jnp.broadcast_to(jnp.sum(inv_own), (1, vectors)),
        ],
        axis=0,
    )
    packed = jnp.concatenate([basis_own, inv_own], axis=1)
    cols_all, rows_all, first = gather_groups(packed, first)
    lang_now = first[:langs]
    prior_scale = first[langs, 0] / doc_total
    basis_cols, inv_cols = cols_all[:, :vectors], cols_all[:, vectors:]
    basis_rows, inv_rows = rows_all[:, :vectors], rows_all[:, vectors:]
    for iteration in range(ITERS):
        last = iteration == ITERS - 1
        lang_mean = prior_scale * (lang_now / counts_real[:, None])
        scaled_cols = (inv_cols * basis_cols).astype(jnp.bfloat16)
        scaled_rows = (inv_rows * basis_rows).astype(jnp.bfloat16)
        part_rows, part_cols = apply_tiles(
            affinity_tiles, pick_rows, pick_cols, scaled_rows, scaled_cols, col_blocks
        )
        product_own = to_own(part_rows, part_cols)
        applied_own = inv_own * product_own + jnp.dot(member_own, lang_mean, precision=highest)
        gram_part = jnp.dot(applied_own.T, applied_own, precision=highest)
        if last:
            gram_matrix = butterfly_sum(gram_part)
        else:
            lang_part = jnp.dot(member_own.T, applied_own, precision=highest)
            applied_cols, applied_rows, sums = gather_groups(
                applied_own, jnp.concatenate([gram_part, lang_part], axis=0)
            )
            gram_matrix = sums[:vectors]
        factor = jnp.linalg.cholesky(gram_matrix / doc_total)
        factor_inv = jax.scipy.linalg.solve_triangular(
            factor, jnp.eye(vectors, dtype=jnp.float32), lower=True
        )
        if last:
            basis_own = jnp.dot(applied_own, factor_inv.T, precision=highest)
        else:
            lang_now = jnp.dot(sums[vectors:], factor_inv.T, precision=highest)
            basis_cols = jnp.dot(applied_cols, factor_inv.T, precision=highest)
            basis_rows = jnp.dot(applied_rows, factor_inv.T, precision=highest)
    return basis_own[None]


def solution(mesh):
    plan = make_plan(mesh.shape["row"], mesh.shape["col"])
    in_specs = (
        P(("row", "col"), None, None),
        P(("row", "col")),
        P(("row", "col")),
        P(),
        P("col", "row", None),
    )
    out_specs = P("col", "row", None)

    def body(*args):
        return shards(*args, plan)

    return jax.shard_map(body, mesh=mesh, in_specs=in_specs, out_specs=out_specs, check_vma=False)
```

```python
import jax
import jax.numpy as jnp
from jax import lax
from jax.sharding import PartitionSpec as P

ROW_BLOCKS = 2
ITERS = 3


highest = lax.Precision.HIGHEST


def membership(first_doc, doc_count, lang_ends, lang_starts):
    doc_index = first_doc + jnp.arange(doc_count, dtype=jnp.int32)
    return (
        (doc_index[:, None] >= lang_starts[None, :]) & (doc_index[:, None] < lang_ends[None, :])
    ).astype(jnp.float32)


def apply_tiles(affinity_tiles, pick_rows, pick_cols, scaled_rows, scaled_cols, col_blocks):
    slot_count, tile_size, _ = affinity_tiles.shape
    vectors = scaled_cols.shape[1]
    blocks_r = scaled_rows.reshape(ROW_BLOCKS, tile_size, vectors)
    blocks_c = scaled_cols.reshape(col_blocks, tile_size, vectors)
    chosen_c = jnp.einsum(
        "tq,qjk->tjk", pick_cols, blocks_c, preferred_element_type=jnp.float32
    ).astype(jnp.bfloat16)
    chosen_r = jnp.einsum(
        "tp,pik->tik", pick_rows, blocks_r, preferred_element_type=jnp.float32
    ).astype(jnp.bfloat16)
    forward = jnp.einsum(
        "tij,tjk->tik", affinity_tiles, chosen_c, preferred_element_type=jnp.float32
    )
    backward = jnp.einsum(
        "tij,tik->tjk", affinity_tiles, chosen_r, preferred_element_type=jnp.float32
    )
    part_rows = jnp.einsum("tp,tik->pik", pick_rows.astype(jnp.float32), forward, precision=highest)
    part_cols = jnp.einsum(
        "tq,tjk->qjk", pick_cols.astype(jnp.float32), backward, precision=highest
    )
    return (
        part_rows.reshape(ROW_BLOCKS * tile_size, vectors),
        part_cols.reshape(col_blocks * tile_size, vectors),
    )


def make_plan(rows, cols):
    group_ratio = rows // cols
    both = ("row", "col")

    def linear(r, c):
        return r * cols + c

    owner_pairs = [
        (linear(r, c), linear((r % group_ratio) * cols + c, r // group_ratio))
        for r in range(rows)
        for c in range(cols)
    ]
    back_pairs = [(dst, src) for src, dst in owner_pairs]

    def to_owner(x):
        return lax.ppermute(x, both, owner_pairs)

    def from_owner(x):
        return lax.ppermute(x, both, back_pairs)

    def halving_scatter(x, axis, size):
        me = lax.axis_index(axis)
        bits = size.bit_length() - 1
        block = x.shape[0] // size
        rest = x.shape[1:]
        x = x.reshape((2,) * bits + (block,) + rest)
        for bit in range(bits):
            place = bits - 1 - bit
            mine = (me >> bit) & 1
            keep = lax.dynamic_index_in_dim(x, mine, axis=place, keepdims=False)
            send = lax.dynamic_index_in_dim(x, 1 - mine, axis=place, keepdims=False)
            pairs = [(i, i ^ (1 << bit)) for i in range(size)]
            x = keep + lax.ppermute(send, axis, pairs)
        return x.reshape((block,) + rest)

    def contiguous_scatter(x, axis, size):
        me = lax.axis_index(axis)
        block = x.shape[0] // size
        dist = size // 2
        while dist >= 1:
            upper = (me // dist) % 2
            keep = lax.dynamic_slice_in_dim(x, upper * dist * block, dist * block, 0)
            send = lax.dynamic_slice_in_dim(x, (1 - upper) * dist * block, dist * block, 0)
            pairs = [(i, i ^ dist) for i in range(size)]
            x = keep + lax.ppermute(send, axis, pairs)
            dist //= 2
        return x

    def doubling_gather(x, axis, size):
        me = lax.axis_index(axis)
        bits = size.bit_length() - 1
        block = x.shape[0]
        rest = x.shape[1:]
        for step in range(bits):
            bit = bits - 1 - step
            upper = ((me >> bit) & 1) == 1
            pairs = [(i, i ^ (1 << bit)) for i in range(size)]
            other = lax.ppermute(x, axis, pairs)
            low = jnp.where(upper, other, x)
            high = jnp.where(upper, x, other)
            x = jnp.stack([low, high], axis=step)
        return x.reshape((size * block,) + rest)

    def butterfly_sum(x):
        total = rows * cols
        me = lax.axis_index("row") * cols + lax.axis_index("col")
        shift = 0
        while (1 << shift) < total:
            if (4 << shift) <= total:
                digit = (me >> shift) % 4
                got = [x]
                for step in (1, 2, 3):
                    pairs = []
                    for i in range(total):
                        d = (i >> shift) % 4
                        j = i - (d << shift) + (((d - step) % 4) << shift)
                        pairs.append((i, j))
                    got.append(lax.ppermute(x, both, pairs))
                stacked = jnp.stack(got)
                by_digit = [
                    lax.dynamic_index_in_dim(stacked, (k - digit) % 4, 0, keepdims=False)
                    for k in range(4)
                ]
                x = (by_digit[0] + by_digit[1]) + (by_digit[2] + by_digit[3])
                shift += 2
            else:
                pairs = [(i, i ^ (1 << shift)) for i in range(total)]
                x = x + lax.ppermute(x, both, pairs)
                shift += 1
        return x

    return to_owner, from_owner, halving_scatter, contiguous_scatter, doubling_gather, butterfly_sum


def shards(affinity_tiles, tile_rows, tile_cols, lang_counts, start_basis, plan):
    to_owner, from_owner, halving_scatter, contiguous_scatter, doubling_gather, butterfly_sum = plan
    row_devices = lax.axis_size("row")
    col_devices = lax.axis_size("col")
    col_blocks = ROW_BLOCKS * row_devices // col_devices
    tile_size = affinity_tiles.shape[1]
    piece_rows = start_basis.shape[1]
    vectors = start_basis.shape[2]
    doc_total = piece_rows * row_devices * col_devices
    my_row = lax.axis_index("row")
    my_col = lax.axis_index("col")
    col_span = col_blocks * tile_size
    piece_offset = my_row * piece_rows
    present = tile_rows >= 0
    local_p = tile_rows - my_row * ROW_BLOCKS
    local_q = tile_cols - my_col * col_blocks
    pick_rows = (
        (local_p[:, None] == jnp.arange(ROW_BLOCKS, dtype=jnp.int32)[None, :]) & present[:, None]
    ).astype(jnp.bfloat16)
    pick_cols = (
        (local_q[:, None] == jnp.arange(col_blocks, dtype=jnp.int32)[None, :]) & present[:, None]
    ).astype(jnp.bfloat16)

    def to_own(rows_part, cols_part):
        from_cols = contiguous_scatter(cols_part, "row", row_devices)
        from_rows = to_owner(halving_scatter(rows_part, "col", col_devices))
        return from_cols + from_rows

    def gather_groups(own):
        cols_all = doubling_gather(own, "row", row_devices)
        rows_all = doubling_gather(from_owner(own), "col", col_devices)
        return cols_all, rows_all

    magnitude = jnp.abs(affinity_tiles)
    row_mass = jnp.sum(magnitude, axis=2, dtype=jnp.float32)
    col_mass = jnp.sum(magnitude, axis=1, dtype=jnp.float32)
    degree_rows = jnp.einsum(
        "tp,ti->pi", pick_rows.astype(jnp.float32), row_mass, precision=highest
    ).reshape(ROW_BLOCKS * tile_size, 1)
    degree_cols = jnp.einsum(
        "tq,tj->qj", pick_cols.astype(jnp.float32), col_mass, precision=highest
    ).reshape(col_span, 1)
    inv_own = lax.rsqrt(1.0 + to_own(degree_rows, degree_cols))
    lang_ends = jnp.cumsum(lang_counts)
    lang_starts = lang_ends - lang_counts
    counts_real = lang_counts.astype(jnp.float32)
    member_own = membership(my_col * col_span + piece_offset, piece_rows, lang_ends, lang_starts)
    basis_own = start_basis[0]
    langs = member_own.shape[1]
    first = jnp.concatenate(
        [
            jnp.dot(member_own.T, basis_own, precision=highest),
            jnp.broadcast_to(jnp.sum(inv_own), (1, vectors)),
        ],
        axis=0,
    )
    packed = jnp.concatenate([basis_own, inv_own], axis=1)
    cols_all, rows_all = gather_groups(packed)
    first = butterfly_sum(first)
    lang_now = first[:langs]
    prior_scale = first[langs, 0] / doc_total
    basis_cols, inv_cols = cols_all[:, :vectors], cols_all[:, vectors:]
    basis_rows, inv_rows = rows_all[:, :vectors], rows_all[:, vectors:]
    for iteration in range(ITERS):
        last = iteration == ITERS - 1
        lang_mean = prior_scale * (lang_now / counts_real[:, None])
        scaled_cols = (inv_cols * basis_cols).astype(jnp.bfloat16)
        scaled_rows = (inv_rows * basis_rows).astype(jnp.bfloat16)
        part_rows, part_cols = apply_tiles(
            affinity_tiles, pick_rows, pick_cols, scaled_rows, scaled_cols, col_blocks
        )
        product_own = to_own(part_rows, part_cols)
        applied_own = inv_own * product_own + jnp.dot(member_own, lang_mean, precision=highest)
        gram_part = jnp.dot(applied_own.T, applied_own, precision=highest)
        if last:
            gram_matrix = butterfly_sum(gram_part)
        else:
            lang_part = jnp.dot(member_own.T, applied_own, precision=highest)
            sums = butterfly_sum(jnp.concatenate([gram_part, lang_part], axis=0))
            gram_matrix = sums[:vectors]
            applied_cols, applied_rows = gather_groups(applied_own)
        factor = jnp.linalg.cholesky(gram_matrix / doc_total)
        factor_inv = jax.scipy.linalg.solve_triangular(
            factor, jnp.eye(vectors, dtype=jnp.float32), lower=True
        )
        if last:
            basis_own = jnp.dot(applied_own, factor_inv.T, precision=highest)
        else:
            lang_now = jnp.dot(sums[vectors:], factor_inv.T, precision=highest)
            basis_cols = jnp.dot(applied_cols, factor_inv.T, precision=highest)
            basis_rows = jnp.dot(applied_rows, factor_inv.T, precision=highest)
    return basis_own[None]


def solution(mesh):
    plan = make_plan(mesh.shape["row"], mesh.shape["col"])
    in_specs = (
        P(("row", "col"), None, None),
        P(("row", "col")),
        P(("row", "col")),
        P(),
        P("col", "row", None),
    )
    out_specs = P("col", "row", None)

    def body(*args):
        return shards(*args, plan)

    return jax.shard_map(body, mesh=mesh, in_specs=in_specs, out_specs=out_specs, check_vma=False)
```

```python
import jax
import jax.numpy as jnp
from jax import lax
from jax.sharding import PartitionSpec as P

ROW_BLOCKS = 2
ITERS = 3


highest = lax.Precision.HIGHEST


def membership(first_doc, doc_count, lang_ends, lang_starts):
    doc_index = first_doc + jnp.arange(doc_count, dtype=jnp.int32)
    return (
        (doc_index[:, None] >= lang_starts[None, :]) & (doc_index[:, None] < lang_ends[None, :])
    ).astype(jnp.float32)


def apply_tiles(affinity_tiles, pick_rows, pick_cols, scaled_rows, scaled_cols, col_blocks):
    slot_count, tile_size, _ = affinity_tiles.shape
    vectors = scaled_cols.shape[1]
    blocks_r = scaled_rows.reshape(ROW_BLOCKS, tile_size, vectors)
    blocks_c = scaled_cols.reshape(col_blocks, tile_size, vectors)
    chosen_c = jnp.einsum(
        "tq,qjk->tjk", pick_cols, blocks_c, preferred_element_type=jnp.float32
    ).astype(jnp.bfloat16)
    chosen_r = jnp.einsum(
        "tp,pik->tik", pick_rows, blocks_r, preferred_element_type=jnp.float32
    ).astype(jnp.bfloat16)
    forward = jnp.einsum(
        "tij,tjk->tik", affinity_tiles, chosen_c, preferred_element_type=jnp.float32
    )
    backward = jnp.einsum(
        "tij,tik->tjk", affinity_tiles, chosen_r, preferred_element_type=jnp.float32
    )
    part_rows = jnp.einsum("tp,tik->pik", pick_rows.astype(jnp.float32), forward, precision=highest)
    part_cols = jnp.einsum(
        "tq,tjk->qjk", pick_cols.astype(jnp.float32), backward, precision=highest
    )
    return (
        part_rows.reshape(ROW_BLOCKS * tile_size, vectors),
        part_cols.reshape(col_blocks * tile_size, vectors),
    )


def make_plan(rows, cols):
    group_ratio = rows // cols
    both = ("row", "col")

    def linear(r, c):
        return r * cols + c

    owner_pairs = [
        (linear(r, c), linear((r % group_ratio) * cols + c, r // group_ratio))
        for r in range(rows)
        for c in range(cols)
    ]
    back_pairs = [(dst, src) for src, dst in owner_pairs]

    def to_owner(x):
        return lax.ppermute(x, both, owner_pairs)

    def from_owner(x):
        return lax.ppermute(x, both, back_pairs)

    def bit_order(axis, size):
        order = list(range(size.bit_length() - 1))
        if axis == "row" and len(order) >= 3:
            order[1], order[2] = order[2], order[1]
        return order

    def halving_scatter(x, axis, size):
        me = lax.axis_index(axis)
        order = bit_order(axis, size)
        bits = len(order)
        block = x.shape[0] // size
        rest = x.shape[1:]
        x = x.reshape((2,) * bits + (block,) + rest)
        left = list(range(bits))
        for bit in order:
            place = sum(1 for other in left if other > bit)
            left.remove(bit)
            mine = (me >> bit) & 1
            keep = lax.dynamic_index_in_dim(x, mine, axis=place, keepdims=False)
            send = lax.dynamic_index_in_dim(x, 1 - mine, axis=place, keepdims=False)
            pairs = [(i, i ^ (1 << bit)) for i in range(size)]
            x = keep + lax.ppermute(send, axis, pairs)
        return x.reshape((block,) + rest)

    def doubling_gather(x, axis, size):
        me = lax.axis_index(axis)
        block = x.shape[0]
        rest = x.shape[1:]
        done = []
        for bit in reversed(bit_order(axis, size)):
            place = sum(1 for other in done if other > bit)
            done.append(bit)
            upper = ((me >> bit) & 1) == 1
            pairs = [(i, i ^ (1 << bit)) for i in range(size)]
            other = lax.ppermute(x, axis, pairs)
            low = jnp.where(upper, other, x)
            high = jnp.where(upper, x, other)
            x = jnp.stack([low, high], axis=place)
        return x.reshape((size * block,) + rest)

    def butterfly_sum(x):
        total = rows * cols
        me = lax.axis_index("row") * cols + lax.axis_index("col")
        shift = 0
        while (1 << shift) < total:
            if (4 << shift) <= total:
                digit = (me >> shift) % 4
                got = [x]
                for step in (1, 2, 3):
                    pairs = []
                    for i in range(total):
                        d = (i >> shift) % 4
                        j = i - (d << shift) + (((d - step) % 4) << shift)
                        pairs.append((i, j))
                    got.append(lax.ppermute(x, both, pairs))
                stacked = jnp.stack(got)
                by_digit = [
                    lax.dynamic_index_in_dim(stacked, (k - digit) % 4, 0, keepdims=False)
                    for k in range(4)
                ]
                x = (by_digit[0] + by_digit[1]) + (by_digit[2] + by_digit[3])
                shift += 2
            else:
                pairs = [(i, i ^ (1 << shift)) for i in range(total)]
                x = x + lax.ppermute(x, both, pairs)
                shift += 1
        return x

    return to_owner, from_owner, halving_scatter, doubling_gather, butterfly_sum


def shards(affinity_tiles, tile_rows, tile_cols, lang_counts, start_basis, plan):
    to_owner, from_owner, halving_scatter, doubling_gather, butterfly_sum = plan
    row_devices = lax.axis_size("row")
    col_devices = lax.axis_size("col")
    col_blocks = ROW_BLOCKS * row_devices // col_devices
    tile_size = affinity_tiles.shape[1]
    piece_rows = start_basis.shape[1]
    vectors = start_basis.shape[2]
    doc_total = piece_rows * row_devices * col_devices
    my_row = lax.axis_index("row")
    my_col = lax.axis_index("col")
    col_span = col_blocks * tile_size
    piece_offset = my_row * piece_rows
    present = tile_rows >= 0
    local_p = tile_rows - my_row * ROW_BLOCKS
    local_q = tile_cols - my_col * col_blocks
    pick_rows = (
        (local_p[:, None] == jnp.arange(ROW_BLOCKS, dtype=jnp.int32)[None, :]) & present[:, None]
    ).astype(jnp.bfloat16)
    pick_cols = (
        (local_q[:, None] == jnp.arange(col_blocks, dtype=jnp.int32)[None, :]) & present[:, None]
    ).astype(jnp.bfloat16)

    def to_own(rows_part, cols_part):
        from_cols = halving_scatter(cols_part, "row", row_devices)
        from_rows = to_owner(halving_scatter(rows_part, "col", col_devices))
        return from_cols + from_rows

    def gather_groups(own):
        cols_all = doubling_gather(own, "row", row_devices)
        rows_all = doubling_gather(from_owner(own), "col", col_devices)
        return cols_all, rows_all

    magnitude = jnp.abs(affinity_tiles)
    row_mass = jnp.sum(magnitude, axis=2, dtype=jnp.float32)
    col_mass = jnp.sum(magnitude, axis=1, dtype=jnp.float32)
    degree_rows = jnp.einsum(
        "tp,ti->pi", pick_rows.astype(jnp.float32), row_mass, precision=highest
    ).reshape(ROW_BLOCKS * tile_size, 1)
    degree_cols = jnp.einsum(
        "tq,tj->qj", pick_cols.astype(jnp.float32), col_mass, precision=highest
    ).reshape(col_span, 1)
    inv_own = lax.rsqrt(1.0 + to_own(degree_rows, degree_cols))
    lang_ends = jnp.cumsum(lang_counts)
    lang_starts = lang_ends - lang_counts
    counts_real = lang_counts.astype(jnp.float32)
    member_own = membership(my_col * col_span + piece_offset, piece_rows, lang_ends, lang_starts)
    basis_own = start_basis[0]
    langs = member_own.shape[1]
    first = jnp.concatenate(
        [
            jnp.dot(member_own.T, basis_own, precision=highest),
            jnp.broadcast_to(jnp.sum(inv_own), (1, vectors)),
        ],
        axis=0,
    )
    packed = jnp.concatenate([basis_own, inv_own], axis=1)
    cols_all, rows_all = gather_groups(packed)
    first = butterfly_sum(first)
    lang_now = first[:langs]
    prior_scale = first[langs, 0] / doc_total
    basis_cols, inv_cols = cols_all[:, :vectors], cols_all[:, vectors:]
    basis_rows, inv_rows = rows_all[:, :vectors], rows_all[:, vectors:]
    for iteration in range(ITERS):
        last = iteration == ITERS - 1
        lang_mean = prior_scale * (lang_now / counts_real[:, None])
        scaled_cols = (inv_cols * basis_cols).astype(jnp.bfloat16)
        scaled_rows = (inv_rows * basis_rows).astype(jnp.bfloat16)
        part_rows, part_cols = apply_tiles(
            affinity_tiles, pick_rows, pick_cols, scaled_rows, scaled_cols, col_blocks
        )
        product_own = to_own(part_rows, part_cols)
        applied_own = inv_own * product_own + jnp.dot(member_own, lang_mean, precision=highest)
        gram_part = jnp.dot(applied_own.T, applied_own, precision=highest)
        if last:
            gram_matrix = butterfly_sum(gram_part)
        else:
            lang_part = jnp.dot(member_own.T, applied_own, precision=highest)
            sums = butterfly_sum(jnp.concatenate([gram_part, lang_part], axis=0))
            gram_matrix = sums[:vectors]
            applied_cols, applied_rows = gather_groups(applied_own)
        factor = jnp.linalg.cholesky(gram_matrix / doc_total)
        factor_inv = jax.scipy.linalg.solve_triangular(
            factor, jnp.eye(vectors, dtype=jnp.float32), lower=True
        )
        if last:
            basis_own = jnp.dot(applied_own, factor_inv.T, precision=highest)
        else:
            lang_now = jnp.dot(sums[vectors:], factor_inv.T, precision=highest)
            basis_cols = jnp.dot(applied_cols, factor_inv.T, precision=highest)
            basis_rows = jnp.dot(applied_rows, factor_inv.T, precision=highest)
    return basis_own[None]


def solution(mesh):
    plan = make_plan(mesh.shape["row"], mesh.shape["col"])
    in_specs = (
        P(("row", "col"), None, None),
        P(("row", "col")),
        P(("row", "col")),
        P(),
        P("col", "row", None),
    )
    out_specs = P("col", "row", None)

    def body(*args):
        return shards(*args, plan)

    return jax.shard_map(body, mesh=mesh, in_specs=in_specs, out_specs=out_specs, check_vma=False)
```

```python
import jax
import jax.numpy as jnp
from jax import lax
from jax.sharding import PartitionSpec as P

ROW_BLOCKS = 2
ITERS = 3


highest = lax.Precision.HIGHEST


def membership(first_doc, doc_count, lang_ends, lang_starts):
    doc_index = first_doc + jnp.arange(doc_count, dtype=jnp.int32)
    return (
        (doc_index[:, None] >= lang_starts[None, :]) & (doc_index[:, None] < lang_ends[None, :])
    ).astype(jnp.float32)


def apply_tiles(affinity_tiles, pick_rows, pick_cols, scaled_rows, scaled_cols, col_blocks):
    slot_count, tile_size, _ = affinity_tiles.shape
    vectors = scaled_cols.shape[1]
    blocks_r = scaled_rows.reshape(ROW_BLOCKS, tile_size, vectors)
    blocks_c = scaled_cols.reshape(col_blocks, tile_size, vectors)
    chosen_c = jnp.einsum(
        "tq,qjk->tjk", pick_cols, blocks_c, preferred_element_type=jnp.float32
    ).astype(jnp.bfloat16)
    chosen_r = jnp.einsum(
        "tp,pik->tik", pick_rows, blocks_r, preferred_element_type=jnp.float32
    ).astype(jnp.bfloat16)
    forward = jnp.einsum(
        "tij,tjk->tik", affinity_tiles, chosen_c, preferred_element_type=jnp.float32
    )
    backward = jnp.einsum(
        "tij,tik->tjk", affinity_tiles, chosen_r, preferred_element_type=jnp.float32
    )
    part_rows = jnp.einsum("tp,tik->pik", pick_rows.astype(jnp.float32), forward, precision=highest)
    part_cols = jnp.einsum(
        "tq,tjk->qjk", pick_cols.astype(jnp.float32), backward, precision=highest
    )
    return (
        part_rows.reshape(ROW_BLOCKS * tile_size, vectors),
        part_cols.reshape(col_blocks * tile_size, vectors),
    )


def make_plan(rows, cols):
    group_ratio = rows // cols
    both = ("row", "col")

    def linear(r, c):
        return r * cols + c

    owner_pairs = [
        (linear(r, c), linear((r % group_ratio) * cols + c, r // group_ratio))
        for r in range(rows)
        for c in range(cols)
    ]
    back_pairs = [(dst, src) for src, dst in owner_pairs]

    def to_owner(x):
        return lax.ppermute(x, both, owner_pairs)

    def from_owner(x):
        return lax.ppermute(x, both, back_pairs)

    def halving_scatter(x, axis, size):
        me = lax.axis_index(axis)
        bits = size.bit_length() - 1
        block = x.shape[0] // size
        rest = x.shape[1:]
        x = x.reshape((2,) * bits + (block,) + rest)
        for bit in range(bits):
            place = bits - 1 - bit
            mine = (me >> bit) & 1
            keep = lax.dynamic_index_in_dim(x, mine, axis=place, keepdims=False)
            send = lax.dynamic_index_in_dim(x, 1 - mine, axis=place, keepdims=False)
            pairs = [(i, i ^ (1 << bit)) for i in range(size)]
            x = keep + lax.ppermute(send, axis, pairs)
        return x.reshape((block,) + rest)

    def doubling_gather(x, axis, size):
        me = lax.axis_index(axis)
        bits = size.bit_length() - 1
        block = x.shape[0]
        rest = x.shape[1:]
        for step in range(bits):
            bit = bits - 1 - step
            upper = ((me >> bit) & 1) == 1
            pairs = [(i, i ^ (1 << bit)) for i in range(size)]
            other = lax.ppermute(x, axis, pairs)
            low = jnp.where(upper, other, x)
            high = jnp.where(upper, x, other)
            x = jnp.stack([low, high], axis=step)
        return x.reshape((size * block,) + rest)

    def butterfly_sum(x):
        total = rows * cols
        me = lax.axis_index("row") * cols + lax.axis_index("col")
        shift = 0
        while (1 << shift) < total:
            if (4 << shift) <= total:
                digit = (me >> shift) % 4
                got = [x]
                for step in (1, 2, 3):
                    pairs = []
                    for i in range(total):
                        d = (i >> shift) % 4
                        j = i - (d << shift) + (((d - step) % 4) << shift)
                        pairs.append((i, j))
                    got.append(lax.ppermute(x, both, pairs))
                stacked = jnp.stack(got)
                by_digit = [
                    lax.dynamic_index_in_dim(stacked, (k - digit) % 4, 0, keepdims=False)
                    for k in range(4)
                ]
                x = (by_digit[0] + by_digit[1]) + (by_digit[2] + by_digit[3])
                shift += 2
            else:
                pairs = [(i, i ^ (1 << shift)) for i in range(total)]
                x = x + lax.ppermute(x, both, pairs)
                shift += 1
        return x

    return to_owner, from_owner, halving_scatter, doubling_gather, butterfly_sum


def shards(affinity_tiles, tile_rows, tile_cols, lang_counts, start_basis, plan):
    to_owner, from_owner, halving_scatter, doubling_gather, butterfly_sum = plan
    row_devices = lax.axis_size("row")
    col_devices = lax.axis_size("col")
    col_blocks = ROW_BLOCKS * row_devices // col_devices
    tile_size = affinity_tiles.shape[1]
    piece_rows = start_basis.shape[1]
    vectors = start_basis.shape[2]
    doc_total = piece_rows * row_devices * col_devices
    my_row = lax.axis_index("row")
    my_col = lax.axis_index("col")
    col_span = col_blocks * tile_size
    piece_offset = my_row * piece_rows
    present = tile_rows >= 0
    local_p = tile_rows - my_row * ROW_BLOCKS
    local_q = tile_cols - my_col * col_blocks
    pick_rows = (
        (local_p[:, None] == jnp.arange(ROW_BLOCKS, dtype=jnp.int32)[None, :]) & present[:, None]
    ).astype(jnp.bfloat16)
    pick_cols = (
        (local_q[:, None] == jnp.arange(col_blocks, dtype=jnp.int32)[None, :]) & present[:, None]
    ).astype(jnp.bfloat16)

    def to_own(rows_part, cols_part):
        from_cols = halving_scatter(cols_part, "row", row_devices)
        from_rows = to_owner(halving_scatter(rows_part, "col", col_devices))
        return from_cols + from_rows

    def gather_groups(own):
        cols_all = doubling_gather(own, "row", row_devices)
        rows_all = doubling_gather(from_owner(own), "col", col_devices)
        return cols_all, rows_all

    magnitude = jnp.abs(affinity_tiles)
    row_mass = jnp.sum(magnitude, axis=2, dtype=jnp.float32)
    col_mass = jnp.sum(magnitude, axis=1, dtype=jnp.float32)
    degree_rows = jnp.einsum(
        "tp,ti->pi", pick_rows.astype(jnp.float32), row_mass, precision=highest
    ).reshape(ROW_BLOCKS * tile_size, 1)
    degree_cols = jnp.einsum(
        "tq,tj->qj", pick_cols.astype(jnp.float32), col_mass, precision=highest
    ).reshape(col_span, 1)
    inv_own = lax.rsqrt(1.0 + to_own(degree_rows, degree_cols))
    lang_ends = jnp.cumsum(lang_counts)
    lang_starts = lang_ends - lang_counts
    counts_real = lang_counts.astype(jnp.float32)
    member_own = membership(my_col * col_span + piece_offset, piece_rows, lang_ends, lang_starts)
    basis_own = start_basis[0]
    langs = member_own.shape[1]
    first = jnp.concatenate(
        [
            jnp.dot(member_own.T, basis_own, precision=highest),
            jnp.broadcast_to(jnp.sum(inv_own), (1, vectors)),
        ],
        axis=0,
    )
    basis_cols, basis_rows = gather_groups(basis_own)
    inv_cols, inv_rows = gather_groups(inv_own.reshape(1, piece_rows))
    inv_cols = inv_cols.reshape(col_span, 1)
    inv_rows = inv_rows.reshape(ROW_BLOCKS * tile_size, 1)
    first = butterfly_sum(first)
    lang_now = first[:langs]
    prior_scale = first[langs, 0] / doc_total
    for iteration in range(ITERS):
        last = iteration == ITERS - 1
        lang_mean = prior_scale * (lang_now / counts_real[:, None])
        scaled_cols = (inv_cols * basis_cols).astype(jnp.bfloat16)
        scaled_rows = (inv_rows * basis_rows).astype(jnp.bfloat16)
        part_rows, part_cols = apply_tiles(
            affinity_tiles, pick_rows, pick_cols, scaled_rows, scaled_cols, col_blocks
        )
        product_own = to_own(part_rows, part_cols)
        applied_own = inv_own * product_own + jnp.dot(member_own, lang_mean, precision=highest)
        gram_part = jnp.dot(applied_own.T, applied_own, precision=highest)
        if last:
            gram_matrix = butterfly_sum(gram_part)
        else:
            lang_part = jnp.dot(member_own.T, applied_own, precision=highest)
            sums = butterfly_sum(jnp.concatenate([gram_part, lang_part], axis=0))
            gram_matrix = sums[:vectors]
            applied_cols, applied_rows = gather_groups(applied_own)
        factor = jnp.linalg.cholesky(gram_matrix / doc_total)
        factor_inv = jax.scipy.linalg.solve_triangular(
            factor, jnp.eye(vectors, dtype=jnp.float32), lower=True
        )
        if last:
            basis_own = jnp.dot(applied_own, factor_inv.T, precision=highest)
        else:
            lang_now = jnp.dot(sums[vectors:], factor_inv.T, precision=highest)
            basis_cols = jnp.dot(applied_cols, factor_inv.T, precision=highest)
            basis_rows = jnp.dot(applied_rows, factor_inv.T, precision=highest)
    return basis_own[None]


def solution(mesh):
    plan = make_plan(mesh.shape["row"], mesh.shape["col"])
    in_specs = (
        P(("row", "col"), None, None),
        P(("row", "col")),
        P(("row", "col")),
        P(),
        P("col", "row", None),
    )
    out_specs = P("col", "row", None)

    def body(*args):
        return shards(*args, plan)

    return jax.shard_map(body, mesh=mesh, in_specs=in_specs, out_specs=out_specs, check_vma=False)
```
